256 devices in a mesh: graph: 8 (over z), index: 32 (over x, y, core).
Axes of the slice: x: 4, y: 4, z: 8, core: 2. Of those that a mesh axis runs over, the one named last changes fastest.
Arguments:
- features: bfloat16 [65536, 1024], P(('graph', 'index')), may hold values from -6 to 6
- q_weight: bfloat16 [1024, 1024], replicated, may hold values from -0.1875 to 0.1875
- q_bias: float32 [1024], replicated, may hold values from -3 to 3
- w_self: bfloat16 [1024, 1024], replicated, may hold values from -0.125 to 0.125
- w_neigh: bfloat16 [1024, 1024], replicated, may hold values from -0.125 to 0.125
- z_bias: float32 [1024], replicated, may hold values from -3 to 3
- centroids: bfloat16 [8192, 1024], P('index'), may hold values from -0.1875 to 0.1875
- requests: int32 [256, 32, 16], P(('graph', 'index')), may hold values from 0 to 255, as said below
- slots: int32 [65536, 50], P(('graph', 'index')), may hold values from 0 to 511
- importance: float32 [65536, 50], P(('graph', 'index')), may hold values from 0.1 to 10
- labels: int32 [65536, 1], P(('graph', 'index')), may hold values from 0 to 31; in each aligned block of 256 rows (0 to 255, 256 to 511, ...) at most 16 rows name the same one
Outputs:
- scores: bfloat16 [65536, 256], P(('graph', 'index'))
The draws below stay inside these ranges and needn't reach their ends.
Inputs may be any that keep to these rules, and one draw needn't show every extreme that they name: `requests`: the 16 rows that a device asks of one device are distinct. `labels`: the rows of one device carry any one label at most 16 times.
All inputs are finite; a program needn't handle non-finite values.
Results may differ from the reference program's by a relative error of at most 0.0051.
Values may be sent and summed in bfloat16 or wider, within the bound.
No kernel may reach another device: no remote copies, remote signals or barrier semaphores. Data moves between devices by JAX's collectives and lax.ppermute only.
A program may use at most 64 MiB of HBM per device.

```python
import math
import jax
import jax.numpy as jnp
import numpy as np
from jax import lax

D = 1024
CENTS = 256
NEIGHBORS = 50
ROWS_DEV = 256
PEERS = 32
SOURCES = 256
FETCH_SLOTS = 16
OWNER_SLOTS = 16
NODES = 65536


def draw_requests(key, part):
    total = SOURCES * PEERS
    keys = jax.random.split(jax.random.fold_in(key, 11), total)
    chosen = jax.random.randint(jax.random.fold_in(key, 12), (), 0, total)
    place = jax.random.randint(jax.random.fold_in(key, 13), (), 0, FETCH_SLOTS)
    flags = jnp.arange(total, dtype=jnp.int32) == chosen

    def one_list(sub_key, forced):
        order = jax.random.permutation(sub_key, ROWS_DEV).astype(jnp.int32)
        where_top = jnp.argmax((order == ROWS_DEV - 1).astype(jnp.int32))
        swapped = order.at[where_top].set(order[place]).at[place].set(ROWS_DEV - 1)
        picked = jnp.where(forced, swapped, order)
        return picked[:FETCH_SLOTS]
    lists = jax.vmap(one_list)(keys, flags)
    return lists.reshape(SOURCES, PEERS, FETCH_SLOTS).astype(jnp.int32)


def place_ends(drawn, stream_key, smallest, largest):
    dims = drawn.shape
    spot = [jax.random.randint(jax.random.fold_in(stream_key, axis), (), 0, dims[axis]) for axis in range(len(dims))]
    drawn = drawn.at[tuple(spot)].set(smallest)
    longest = dims.index(max(dims))
    spot[longest] = (spot[longest] + 1) % dims[longest]
    return drawn.at[tuple(spot)].set(largest)


def levels(own_key, dims, cuts, smallest, largest):
    def one(dim, parts):
        heights = jax.random.uniform(jax.random.fold_in(jax.random.fold_in(own_key, 6), dim), (parts,), jnp.float32, smallest / len(cuts), largest / len(cuts))
        return jnp.repeat(jnp.exp(heights), dims[dim] // parts).reshape((-1,) + (1,) * (len(dims) - dim - 1))

    loudness = one(*cuts[0])
    for cut in cuts[1:]:
        loudness = loudness * one(*cut)
    return loudness


def shared_out(rng, own, number, rows, number_of, top, reach, slope):
    sequence = jax.random.permutation(rng, number_of)
    crowded, usual = load_shares(number_of, rows * top, reach, slope, True), load_shares(number_of, rows * top, reach, slope, False)
    places = jnp.arange(number_of)

    def named(lengths, offset_by):
        used = int((lengths > 0).sum())
        fixed = max(1, used // 4)
        shifted = fixed + (places - fixed + offset_by * (used - fixed)) % max(1, number_of - fixed)
        return jnp.zeros((number_of,), jnp.int32).at[sequence[jnp.where(places < fixed, places, shifted)]].set(jnp.asarray(lengths, jnp.int32))

    lengths = jnp.where(number % 4 == 0, named(crowded, number // 4), named(usual, number - number // 4 - 1))
    mixed = jax.random.permutation(jax.random.fold_in(own, 3), number_of)
    source_of, sink = mixed[0:number_of // 2 * 2:2], mixed[1:number_of // 2 * 2:2]
    margin = jnp.minimum(lengths[source_of] - 1, reach - lengths[sink]) // 2
    margin = jnp.where((source_of == sequence[0]) | (sink == sequence[0]) | (lengths[sink] == 0), 0, jnp.maximum(margin, 0))
    shifted = jax.random.randint(jax.random.fold_in(own, 4), (number_of // 2,), 0, 1 << 20) % (margin + 1)
    lengths = lengths.at[source_of].add(-shifted).at[sink].add(shifted)
    items = jnp.searchsorted(jnp.cumsum(lengths), jnp.arange(rows * top), side="right").astype(jnp.int32)
    grid = items.reshape(top, rows).T
    grid = grid[jax.random.permutation(jax.random.fold_in(own, 1), rows)]
    offset_by = jax.random.randint(jax.random.fold_in(own, 2), (rows, 1), 0, top)
    return jnp.take_along_axis(grid, (jnp.arange(top)[None, :] + offset_by) % top, axis=1)


def load_shares(amount, total, limit, slope, full):
    loads = [(1 << 20) // math.isqrt(rank ** slope) + 1 for rank in range(1, amount + 1)]
    largest = limit if full else min(limit, max(-(-total // amount), total * loads[0] // sum(loads)))
    least = 1 if total - largest >= amount - 1 else 0
    given, surplus = [largest] + [least] * (amount - 1), total - largest - least * (amount - 1)
    while surplus > 0:
        candidates = [i for i in range(1, amount) if given[i] < largest] or [i for i in range(1, amount) if given[i] < limit]
        pool, remaining = sum([loads[i] for i in candidates]), surplus
        for i in candidates:
            more = min(limit - given[i], max(1, remaining * loads[i] // pool), surplus)
            given[i] = given[i] + more
            surplus = surplus - more
    return np.array(given)


def centred(own_key, extent, scale, reach, shards=(), held_as=jnp.bfloat16):
    gain = levels(own_key, extent, shards, -0.22, 0.18) if shards else 1.0
    drawn = jax.random.normal(own_key, extent, jnp.float32) * scale * gain
    return jnp.minimum(jnp.maximum(drawn, -reach), reach).astype(held_as)


def setup_inputs(seed: int = 0) -> dict:
    arg_keys = jax.random.split(jax.random.key(seed), 12)
    features = centred(arg_keys[0], (NODES, D), 1.0, 6.0, ((0, 256),))
    q_weight = centred(arg_keys[1], (D, D), D ** -0.5, 0.1875)
    q_bias = centred(arg_keys[2], (D,), 0.5, 3.0, (), jnp.float32)
    w_self = centred(arg_keys[3], (D, D), (2 * D) ** -0.5, 0.125)
    w_neigh = centred(arg_keys[4], (D, D), (2 * D) ** -0.5, 0.125)
    z_bias = centred(arg_keys[5], (D,), 0.5, 3.0, (), jnp.float32)
    centroids = centred(arg_keys[6], (CENTS * PEERS, D), D ** -0.5, 0.1875, ((0, 32),))
    requests = draw_requests(jax.random.fold_in(arg_keys[11], 71), 0)
    slots = place_ends(jax.random.randint(arg_keys[8], (NODES, NEIGHBORS), 0, PEERS * FETCH_SLOTS), jax.random.fold_in(arg_keys[8], 1), 0, (PEERS * FETCH_SLOTS) - 1).astype(jnp.int32)
    importance = jnp.clip(jnp.exp(math.log(10.0) - 4.6051702 * jax.random.uniform(arg_keys[9], (NODES, NEIGHBORS), jnp.float32) ** levels(arg_keys[9], (NODES, NEIGHBORS), ((0, 256),), -0.2, 0.2)), 0.1, 10.0)
    labels_keys = jax.random.split(jax.random.fold_in(arg_keys[10], 1), NODES // ROWS_DEV)
    labels_turns = jax.random.permutation(jax.random.fold_in(arg_keys[10], 3), NODES // ROWS_DEV)
    labels = jax.vmap(lambda own, number: shared_out(jax.random.fold_in(arg_keys[10], 2), own, number, ROWS_DEV, PEERS, 1, OWNER_SLOTS, 2))(labels_keys, labels_turns).reshape((NODES, 1))
    return {"features": features, "q_weight": q_weight, "q_bias": q_bias, "w_self": w_self, "w_neigh": w_neigh, "z_bias": z_bias, "centroids": centroids, "requests": requests, "slots": slots, "importance": importance, "labels": labels}


def place_rows(label_rows):
    hits = (label_rows[:, None] == jnp.arange(PEERS, dtype=jnp.int32)[None, :]).astype(jnp.int32)
    ranks = lax.optimization_barrier(jnp.sum(hits * (jnp.cumsum(hits, axis=0) - 1), axis=1))
    return label_rows * OWNER_SLOTS + ranks

def pool_device(device, messages, requests, slots, weights_norm):
    group_id = device // PEERS
    asked_rows = requests[device]
    owner_ids = group_id * PEERS + jnp.arange(PEERS, dtype=jnp.int32)
    global_rows = (owner_ids[:, None] * ROWS_DEV + asked_rows).reshape(-1)
    fetched = jnp.take(messages, global_rows, axis=0)
    slot_rows = lax.dynamic_slice_in_dim(slots, device * ROWS_DEV, ROWS_DEV, 0)
    weight_rows = lax.dynamic_slice_in_dim(weights_norm, device * ROWS_DEV, ROWS_DEV, 0)
    slot_ids = jnp.arange(PEERS * FETCH_SLOTS, dtype=jnp.int32)
    mixing = lax.optimization_barrier(jnp.sum(jnp.where(slot_rows[:, :, None] == slot_ids[None, None, :], weight_rows[:, :, None], 0.0), axis=1)).astype(jnp.bfloat16)
    return jnp.dot(mixing, fetched, preferred_element_type=jnp.float32).astype(jnp.bfloat16)

def score_device(device, normed, labels, blocks):
    row_block = lax.dynamic_slice_in_dim(normed, device * ROWS_DEV, ROWS_DEV, 0)
    label_rows = lax.dynamic_slice_in_dim(labels, device * ROWS_DEV, ROWS_DEV, 0)[:, 0]
    positions = place_rows(label_rows)
    buffer = jnp.zeros((PEERS * OWNER_SLOTS, normed.shape[1]), normed.dtype).at[positions].set(row_block)
    buffer = buffer.reshape(PEERS, OWNER_SLOTS, normed.shape[1]).astype(jnp.float32)
    raw = jnp.einsum('pcd,pkd->pck', buffer, blocks).astype(jnp.bfloat16)
    return jnp.take(raw.reshape(PEERS * OWNER_SLOTS, CENTS), positions, axis=0)

def reference(features, q_weight, q_bias, w_self, w_neigh, z_bias, centroids, requests, slots, importance, labels):
    width = features.shape[1]
    messages = jax.nn.relu(jnp.dot(features, q_weight, preferred_element_type=jnp.float32) + q_bias).astype(jnp.bfloat16)
    weights_norm = importance / lax.optimization_barrier(jnp.sum(importance, axis=1, keepdims=True))
    device_ids = jnp.arange(SOURCES, dtype=jnp.int32)
    pooled = lax.map(lambda device: pool_device(device, messages, requests, slots, weights_norm), device_ids).reshape(-1, width)
    hidden = jax.nn.relu(jnp.dot(features, w_self, preferred_element_type=jnp.float32) + jnp.dot(pooled, w_neigh, preferred_element_type=jnp.float32) + z_bias)
    normed = (hidden * lax.rsqrt(lax.optimization_barrier(jnp.mean(hidden * hidden, axis=1, keepdims=True)) + 1e-06)).astype(jnp.bfloat16)
    blocks = centroids.astype(jnp.float32).reshape(PEERS, CENTS, width)
    scores = lax.map(lambda device: score_device(device, normed, labels, blocks), device_ids)
    return scores.reshape(-1, CENTS)
```

```python
import jax
import jax.numpy as jnp
from jax import lax
from jax.sharding import PartitionSpec as P


def place_rows(label_rows, peer_count, owner_slots):
    hits = (label_rows[:, None] == jnp.arange(peer_count, dtype=jnp.int32)[None, :]).astype(
        jnp.int32
    )
    ranks = jnp.sum(hits * (jnp.cumsum(hits, axis=0) - 1), axis=1)
    return label_rows * owner_slots + ranks


def body(
    features,
    q_weight,
    q_bias,
    w_self,
    w_neigh,
    z_bias,
    centroids,
    requests,
    slots,
    importance,
    labels,
):
    row_count = features.shape[0]
    width = features.shape[1]
    peer_count = lax.axis_size("index")
    owner_slots = max(2 * row_count // peer_count, 2)
    fetch_slots = requests.shape[2]
    slot_count = peer_count * fetch_slots
    cent_count = centroids.shape[0]
    messages = jax.nn.relu(
        jnp.dot(features, q_weight, preferred_element_type=jnp.float32) + q_bias
    ).astype(jnp.bfloat16)
    weights_norm = importance / jnp.sum(importance, axis=1, keepdims=True)
    slot_ids = jnp.arange(slot_count, dtype=jnp.int32)
    mixing = jnp.sum(
        jnp.where(slots[:, :, None] == slot_ids[None, None, :], weights_norm[:, :, None], 0.0),
        axis=1,
    ).astype(jnp.bfloat16)
    asked_rows = requests[0]
    wanted = lax.all_to_all(asked_rows, "index", split_axis=0, concat_axis=0, tiled=True)
    outgoing_msgs = jnp.take(messages, wanted.reshape(-1), axis=0)
    fetched = lax.all_to_all(
        outgoing_msgs.reshape(peer_count, fetch_slots, width),
        "index",
        split_axis=0,
        concat_axis=0,
        tiled=True,
    ).reshape(slot_count, width)
    pooled = jnp.dot(mixing, fetched, preferred_element_type=jnp.float32).astype(jnp.bfloat16)
    hidden = jax.nn.relu(
        jnp.dot(features, w_self, preferred_element_type=jnp.float32)
        + jnp.dot(pooled, w_neigh, preferred_element_type=jnp.float32)
        + z_bias
    )
    normed = (hidden * lax.rsqrt(jnp.mean(hidden * hidden, axis=1, keepdims=True) + 1e-06)).astype(
        jnp.bfloat16
    )
    positions = place_rows(labels[:, 0], peer_count, owner_slots)
    outgoing = jnp.zeros((peer_count * owner_slots, width), jnp.bfloat16).at[positions].set(normed)
    outgoing = outgoing.reshape(peer_count, owner_slots, width)
    arrived = lax.all_to_all(outgoing, "index", split_axis=0, concat_axis=0, tiled=True)
    flat_rows = arrived.reshape(-1, width)
    raw_scores = lax.dot_general(
        flat_rows, centroids, (((1,), (1,)), ((), ())), preferred_element_type=jnp.float32
    ).astype(jnp.bfloat16)
    returned = lax.all_to_all(
        raw_scores.reshape(peer_count, arrived.shape[1], cent_count),
        "index",
        split_axis=0,
        concat_axis=0,
        tiled=True,
    )
    return jnp.take(returned.reshape(peer_count * owner_slots, cent_count), positions, axis=0)


def solution(mesh):
    return jax.shard_map(
        body,
        mesh=mesh,
        in_specs=(
            P(("graph", "index"), None),
            P(),
            P(),
            P(),
            P(),
            P(),
            P("index", None),
            P(("graph", "index"), None, None),
            P(("graph", "index"), None),
            P(("graph", "index"), None),
            P(("graph", "index"), None),
        ),
        out_specs=P(("graph", "index"), None),
        check_vma=False,
    )
```

```python
import jax
import jax.numpy as jnp
from jax import lax
from jax.sharding import PartitionSpec as P


def place_rows(label_rows, peer_count, owner_slots):
    hits = (label_rows[:, None] == jnp.arange(peer_count, dtype=jnp.int32)[None, :]).astype(
        jnp.int32
    )
    ranks = jnp.sum(hits * (jnp.cumsum(hits, axis=0) - 1), axis=1)
    return label_rows * owner_slots + ranks


def one_hot(index, count):
    return (index[:, None] == jnp.arange(count, dtype=jnp.int32)[None, :]).astype(jnp.bfloat16)


def body(
    features,
    q_weight,
    q_bias,
    w_self,
    w_neigh,
    z_bias,
    centroids,
    requests,
    slots,
    importance,
    labels,
):
    row_count = features.shape[0]
    width = features.shape[1]
    peer_count = lax.axis_size("index")
    owner_slots = max(2 * row_count // peer_count, 2)
    fetch_slots = requests.shape[2]
    slot_count = peer_count * fetch_slots
    cent_count = centroids.shape[0]
    me = lax.axis_index("index")
    all_requests = lax.all_gather(requests[0], "index", axis=0, tiled=False)
    messages = jax.nn.relu(
        jnp.dot(features, q_weight, preferred_element_type=jnp.float32) + q_bias
    ).astype(jnp.bfloat16)
    weights_norm = importance / jnp.sum(importance, axis=1, keepdims=True)
    slot_ids = jnp.arange(slot_count, dtype=jnp.int32)
    mixing = jnp.sum(
        jnp.where(slots[:, :, None] == slot_ids[None, None, :], weights_norm[:, :, None], 0.0),
        axis=1,
    ).astype(jnp.bfloat16)
    wanted = lax.dynamic_index_in_dim(all_requests, me, axis=1, keepdims=False)
    outgoing_msgs = jnp.dot(
        one_hot(wanted.reshape(-1), row_count), messages, preferred_element_type=jnp.float32
    ).astype(jnp.bfloat16)
    fetched = lax.all_to_all(
        outgoing_msgs.reshape(peer_count, fetch_slots, width),
        "index",
        split_axis=0,
        concat_axis=0,
        tiled=True,
    ).reshape(slot_count, width)
    pooled = jnp.dot(mixing, fetched, preferred_element_type=jnp.float32).astype(jnp.bfloat16)
    hidden = jax.nn.relu(
        jnp.dot(features, w_self, preferred_element_type=jnp.float32)
        + jnp.dot(pooled, w_neigh, preferred_element_type=jnp.float32)
        + z_bias
    )
    normed = (hidden * lax.rsqrt(jnp.mean(hidden * hidden, axis=1, keepdims=True) + 1e-06)).astype(
        jnp.bfloat16
    )
    positions = place_rows(labels[:, 0], peer_count, owner_slots)
    pick = one_hot(positions, peer_count * owner_slots)
    outgoing = lax.dot_general(
        pick, normed, (((0,), (0,)), ((), ())), preferred_element_type=jnp.float32
    ).astype(jnp.bfloat16)
    outgoing = outgoing.reshape(peer_count, owner_slots, width)
    arrived = lax.all_to_all(outgoing, "index", split_axis=0, concat_axis=0, tiled=True)
    flat_rows = arrived.reshape(-1, width)
    raw_scores = lax.dot_general(
        flat_rows, centroids, (((1,), (1,)), ((), ())), preferred_element_type=jnp.float32
    ).astype(jnp.bfloat16)
    returned = lax.all_to_all(
        raw_scores.reshape(peer_count, arrived.shape[1], cent_count),
        "index",
        split_axis=0,
        concat_axis=0,
        tiled=True,
    )
    return jnp.dot(
        pick, returned.reshape(peer_count * owner_slots, cent_count),
        preferred_element_type=jnp.float32,
    ).astype(jnp.bfloat16)


def solution(mesh):
    return jax.shard_map(
        body,
        mesh=mesh,
        in_specs=(
            P(("graph", "index"), None),
            P(),
            P(),
            P(),
            P(),
            P(),
            P("index", None),
            P(("graph", "index"), None, None),
            P(("graph", "index"), None),
            P(("graph", "index"), None),
            P(("graph", "index"), None),
        ),
        out_specs=P(("graph", "index"), None),
        check_vma=False,
    )
```

```python
import jax
import jax.numpy as jnp
from jax import lax
from jax.sharding import PartitionSpec as P


def place_rows(label_rows, peer_count, owner_slots):
    hits = (label_rows[:, None] == jnp.arange(peer_count, dtype=jnp.int32)[None, :]).astype(
        jnp.int32
    )
    ranks = jnp.sum(hits * (jnp.cumsum(hits, axis=0) - 1), axis=1)
    return label_rows * owner_slots + ranks


def one_hot(index, count):
    return (index[:, None] == jnp.arange(count, dtype=jnp.int32)[None, :]).astype(jnp.bfloat16)


def body(
    features,
    q_weight,
    q_bias,
    w_self,
    w_neigh,
    z_bias,
    centroids,
    requests,
    slots,
    importance,
    labels,
):
    row_count = features.shape[0]
    width = features.shape[1]
    peer_count = lax.axis_size("index")
    owner_slots = max(2 * row_count // peer_count, 2)
    fetch_slots = requests.shape[2]
    slot_count = peer_count * fetch_slots
    cent_count = centroids.shape[0]
    wanted = lax.all_to_all(requests, "index", split_axis=1, concat_axis=1, tiled=True)[0]
    messages = jax.nn.relu(
        jnp.dot(features, q_weight, preferred_element_type=jnp.float32) + q_bias
    ).astype(jnp.bfloat16)
    weights_norm = importance / jnp.sum(importance, axis=1, keepdims=True)
    slot_ids = jnp.arange(slot_count, dtype=jnp.int32)
    mixing = jnp.sum(
        jnp.where(slots[:, :, None] == slot_ids[None, None, :], weights_norm[:, :, None], 0.0),
        axis=1,
    ).astype(jnp.bfloat16)
    outgoing_msgs = jnp.dot(
        one_hot(wanted.reshape(-1), row_count), messages, preferred_element_type=jnp.float32
    ).astype(jnp.bfloat16)
    fetched = lax.all_to_all(
        outgoing_msgs.reshape(peer_count, fetch_slots, width),
        "index",
        split_axis=0,
        concat_axis=0,
        tiled=True,
    ).reshape(slot_count, width)
    pooled = jnp.dot(mixing, fetched, preferred_element_type=jnp.float32).astype(jnp.bfloat16)
    hidden = jax.nn.relu(
        jnp.dot(features, w_self, preferred_element_type=jnp.float32)
        + jnp.dot(pooled, w_neigh, preferred_element_type=jnp.float32)
        + z_bias
    )
    normed = (hidden * lax.rsqrt(jnp.mean(hidden * hidden, axis=1, keepdims=True) + 1e-06)).astype(
        jnp.bfloat16
    )
    positions = place_rows(labels[:, 0], peer_count, owner_slots)
    pick = one_hot(positions, peer_count * owner_slots)
    outgoing = lax.dot_general(
        pick, normed, (((0,), (0,)), ((), ())), preferred_element_type=jnp.float32
    ).astype(jnp.bfloat16)
    outgoing = outgoing.reshape(peer_count, owner_slots, width)
    arrived = lax.all_to_all(outgoing, "index", split_axis=0, concat_axis=0, tiled=True)
    flat_rows = arrived.reshape(-1, width)
    raw_scores = lax.dot_general(
        flat_rows, centroids, (((1,), (1,)), ((), ())), preferred_element_type=jnp.float32
    ).astype(jnp.bfloat16)
    returned = lax.all_to_all(
        raw_scores.reshape(peer_count, arrived.shape[1], cent_count),
        "index",
        split_axis=0,
        concat_axis=0,
        tiled=True,
    )
    return jnp.dot(
        pick, returned.reshape(peer_count * owner_slots, cent_count),
        preferred_element_type=jnp.float32,
    ).astype(jnp.bfloat16)


def solution(mesh):
    return jax.shard_map(
        body,
        mesh=mesh,
        in_specs=(
            P(("graph", "index"), None),
            P(),
            P(),
            P(),
            P(),
            P(),
            P("index", None),
            P(("graph", "index"), None, None),
            P(("graph", "index"), None),
            P(("graph", "index"), None),
            P(("graph", "index"), None),
        ),
        out_specs=P(("graph", "index"), None),
        check_vma=False,
    )
```

```python
import jax
import jax.numpy as jnp
from jax import lax
from jax.sharding import PartitionSpec as P


def place_rows(label_rows, peer_count, owner_slots):
    hits = (label_rows[:, None] == jnp.arange(peer_count, dtype=jnp.int32)[None, :]).astype(
        jnp.int32
    )
    ranks = jnp.sum(hits * (jnp.cumsum(hits, axis=0) - 1), axis=1)
    return label_rows * owner_slots + ranks


def one_hot(index, count):
    return (index[:, None] == jnp.arange(count, dtype=jnp.int32)[None, :]).astype(jnp.bfloat16)


def body(
    features,
    q_weight,
    q_bias,
    w_self,
    w_neigh,
    z_bias,
    centroids,
    requests,
    slots,
    importance,
    labels,
):
    row_count = features.shape[0]
    width = features.shape[1]
    peer_count = lax.axis_size("index")
    owner_slots = max(2 * row_count // peer_count, 2)
    fetch_slots = requests.shape[2]
    slot_count = peer_count * fetch_slots
    cent_count = centroids.shape[0]
    wanted = lax.all_to_all(requests, "index", split_axis=1, concat_axis=1, tiled=True)[0]
    messages = jax.nn.relu(
        jnp.dot(features, q_weight, preferred_element_type=jnp.float32) + q_bias
    ).astype(jnp.bfloat16)
    weights_norm = importance / jnp.sum(importance, axis=1, keepdims=True)
    slot_ids = jnp.arange(slot_count, dtype=jnp.int32)
    mixing = jnp.sum(
        jnp.where(slots[:, :, None] == slot_ids[None, None, :], weights_norm[:, :, None], 0.0),
        axis=1,
    ).astype(jnp.bfloat16)
    outgoing_msgs = jnp.dot(
        one_hot(wanted.reshape(-1), row_count),
        lax.optimization_barrier(messages),
        preferred_element_type=jnp.float32,
    ).astype(jnp.bfloat16)
    fetched = lax.all_to_all(
        outgoing_msgs.reshape(peer_count, fetch_slots, width),
        "index",
        split_axis=0,
        concat_axis=0,
        tiled=True,
    ).reshape(slot_count, width)
    pooled = jnp.dot(mixing, fetched, preferred_element_type=jnp.float32).astype(jnp.bfloat16)
    hidden = jax.nn.relu(
        jnp.dot(features, w_self, preferred_element_type=jnp.float32)
        + jnp.dot(pooled, w_neigh, preferred_element_type=jnp.float32)
        + z_bias
    )
    normed = (hidden * lax.rsqrt(jnp.mean(hidden * hidden, axis=1, keepdims=True) + 1e-06)).astype(
        jnp.bfloat16
    )
    positions = place_rows(labels[:, 0], peer_count, owner_slots)
    pick = one_hot(positions, peer_count * owner_slots)
    outgoing = lax.dot_general(
        pick, normed, (((0,), (0,)), ((), ())), preferred_element_type=jnp.float32
    ).astype(jnp.bfloat16)
    outgoing = outgoing.reshape(peer_count, owner_slots, width)
    arrived = lax.all_to_all(outgoing, "index", split_axis=0, concat_axis=0, tiled=True)
    flat_rows = arrived.reshape(-1, width)
    raw_scores = lax.dot_general(
        flat_rows, centroids, (((1,), (1,)), ((), ())), preferred_element_type=jnp.float32
    ).astype(jnp.bfloat16)
    returned = lax.all_to_all(
        raw_scores.reshape(peer_count, arrived.shape[1], cent_count),
        "index",
        split_axis=0,
        concat_axis=0,
        tiled=True,
    )
    return jnp.dot(
        pick, returned.reshape(peer_count * owner_slots, cent_count),
        preferred_element_type=jnp.float32,
    ).astype(jnp.bfloat16)


def solution(mesh):
    return jax.shard_map(
        body,
        mesh=mesh,
        in_specs=(
            P(("graph", "index"), None),
            P(),
            P(),
            P(),
            P(),
            P(),
            P("index", None),
            P(("graph", "index"), None, None),
            P(("graph", "index"), None),
            P(("graph", "index"), None),
            P(("graph", "index"), None),
        ),
        out_specs=P(("graph", "index"), None),
        check_vma=False,
    )
```

```python
import jax
import jax.numpy as jnp
from jax import lax
from jax.sharding import PartitionSpec as P


def place_rows(label_rows, peer_count, owner_slots):
    hits = (label_rows[:, None] == jnp.arange(peer_count, dtype=jnp.int32)[None, :]).astype(
        jnp.int32
    )
    ranks = jnp.sum(hits * (jnp.cumsum(hits, axis=0) - 1), axis=1)
    return label_rows * owner_slots + ranks


def one_hot(index, count):
    return (index[:, None] == jnp.arange(count, dtype=jnp.int32)[None, :]).astype(jnp.bfloat16)


def body(
    features,
    q_weight,
    q_bias,
    w_self,
    w_neigh,
    z_bias,
    centroids,
    requests,
    slots,
    importance,
    labels,
):
    row_count = features.shape[0]
    width = features.shape[1]
    peer_count = lax.axis_size("index")
    owner_slots = max(2 * row_count // peer_count, 2)
    fetch_slots = requests.shape[2]
    slot_count = peer_count * fetch_slots
    cent_count = centroids.shape[0]
    me = lax.axis_index("index")
    own_rows = jnp.where(
        jnp.arange(peer_count, dtype=jnp.int32)[:, None, None] == me,
        requests.astype(jnp.float32),
        0.0,
    )
    all_requests = lax.psum(own_rows, "index")
    wanted = lax.dynamic_index_in_dim(all_requests, me, axis=1, keepdims=False).astype(jnp.int32)
    messages = jax.nn.relu(
        jnp.dot(features, q_weight, preferred_element_type=jnp.float32) + q_bias
    ).astype(jnp.bfloat16)
    weights_norm = importance / jnp.sum(importance, axis=1, keepdims=True)
    slot_ids = jnp.arange(slot_count, dtype=jnp.int32)
    mixing = jnp.sum(
        jnp.where(slots[:, :, None] == slot_ids[None, None, :], weights_norm[:, :, None], 0.0),
        axis=1,
    ).astype(jnp.bfloat16)
    outgoing_msgs = jnp.dot(
        one_hot(wanted.reshape(-1), row_count),
        lax.optimization_barrier(messages),
        preferred_element_type=jnp.float32,
    ).astype(jnp.bfloat16)
    fetched = lax.all_to_all(
        outgoing_msgs.reshape(peer_count, fetch_slots, width),
        "index",
        split_axis=0,
        concat_axis=0,
        tiled=True,
    ).reshape(slot_count, width)
    pooled = jnp.dot(mixing, fetched, preferred_element_type=jnp.float32).astype(jnp.bfloat16)
    hidden = jax.nn.relu(
        jnp.dot(features, w_self, preferred_element_type=jnp.float32)
        + jnp.dot(pooled, w_neigh, preferred_element_type=jnp.float32)
        + z_bias
    )
    normed = (hidden * lax.rsqrt(jnp.mean(hidden * hidden, axis=1, keepdims=True) + 1e-06)).astype(
        jnp.bfloat16
    )
    positions = place_rows(labels[:, 0], peer_count, owner_slots)
    pick = one_hot(positions, peer_count * owner_slots)
    outgoing = lax.dot_general(
        pick, normed, (((0,), (0,)), ((), ())), preferred_element_type=jnp.float32
    ).astype(jnp.bfloat16)
    outgoing = outgoing.reshape(peer_count, owner_slots, width)
    arrived = lax.all_to_all(outgoing, "index", split_axis=0, concat_axis=0, tiled=True)
    flat_rows = arrived.reshape(-1, width)
    raw_scores = lax.dot_general(
        flat_rows, centroids, (((1,), (1,)), ((), ())), preferred_element_type=jnp.float32
    ).astype(jnp.bfloat16)
    returned = lax.all_to_all(
        raw_scores.reshape(peer_count, arrived.shape[1], cent_count),
        "index",
        split_axis=0,
        concat_axis=0,
        tiled=True,
    )
    return jnp.dot(
        pick, returned.reshape(peer_count * owner_slots, cent_count),
        preferred_element_type=jnp.float32,
    ).astype(jnp.bfloat16)


def solution(mesh):
    return jax.shard_map(
        body,
        mesh=mesh,
        in_specs=(
            P(("graph", "index"), None),
            P(),
            P(),
            P(),
            P(),
            P(),
            P("index", None),
            P(("graph", "index"), None, None),
            P(("graph", "index"), None),
            P(("graph", "index"), None),
            P(("graph", "index"), None),
        ),
        out_specs=P(("graph", "index"), None),
        check_vma=False,
    )
```

```python
import jax
import jax.numpy as jnp
from jax import lax
from jax.sharding import PartitionSpec as P


def place_rows(label_rows, peer_count, owner_slots):
    hits = (label_rows[:, None] == jnp.arange(peer_count, dtype=jnp.int32)[None, :]).astype(
        jnp.int32
    )
    ranks = jnp.sum(hits * (jnp.cumsum(hits, axis=0) - 1), axis=1)
    return label_rows * owner_slots + ranks


def one_hot(index, count):
    return (index[:, None] == jnp.arange(count, dtype=jnp.int32)[None, :]).astype(jnp.bfloat16)


def body(
    features,
    q_weight,
    q_bias,
    w_self,
    w_neigh,
    z_bias,
    centroids,
    requests,
    slots,
    importance,
    labels,
):
    row_count = features.shape[0]
    width = features.shape[1]
    peer_count = lax.axis_size("index")
    owner_slots = max(2 * row_count // peer_count, 2)
    fetch_slots = requests.shape[2]
    slot_count = peer_count * fetch_slots
    cent_count = centroids.shape[0]
    wanted = lax.all_to_all(requests.astype(jnp.float32), "index", split_axis=1, concat_axis=1, tiled=True)[0].astype(jnp.int32)
    messages = jax.nn.relu(
        jnp.dot(features, q_weight, preferred_element_type=jnp.float32) + q_bias
    ).astype(jnp.bfloat16)
    weights_norm = importance / jnp.sum(importance, axis=1, keepdims=True)
    slot_ids = jnp.arange(slot_count, dtype=jnp.int32)
    mixing = jnp.sum(
        jnp.where(slots[:, :, None] == slot_ids[None, None, :], weights_norm[:, :, None], 0.0),
        axis=1,
    ).astype(jnp.bfloat16)
    outgoing_msgs = jnp.dot(
        one_hot(wanted.reshape(-1), row_count), messages, preferred_element_type=jnp.float32
    ).astype(jnp.bfloat16)
    fetched = lax.all_to_all(
        outgoing_msgs.reshape(peer_count, fetch_slots, width),
        "index",
        split_axis=0,
        concat_axis=0,
        tiled=True,
    ).reshape(slot_count, width)
    pooled = lax.optimization_barrier(
        jnp.dot(mixing, fetched, preferred_element_type=jnp.float32).astype(jnp.bfloat16))
    hidden = jax.nn.relu(
        jnp.dot(features, w_self, preferred_element_type=jnp.float32)
        + jnp.dot(pooled, w_neigh, preferred_element_type=jnp.float32)
        + z_bias
    )
    normed = (hidden * lax.rsqrt(jnp.mean(hidden * hidden, axis=1, keepdims=True) + 1e-06)).astype(
        jnp.bfloat16
    )
    positions = place_rows(labels[:, 0], peer_count, owner_slots)
    pick = one_hot(positions, peer_count * owner_slots)
    outgoing = lax.dot_general(
        pick, normed, (((0,), (0,)), ((), ())), preferred_element_type=jnp.float32
    ).astype(jnp.bfloat16)
    outgoing = outgoing.reshape(peer_count, owner_slots, width)
    arrived = lax.all_to_all(outgoing, "index", split_axis=0, concat_axis=0, tiled=True)
    flat_rows = arrived.reshape(-1, width)
    raw_scores = lax.dot_general(
        flat_rows, centroids, (((1,), (1,)), ((), ())), preferred_element_type=jnp.float32
    ).astype(jnp.bfloat16)
    returned = lax.all_to_all(
        raw_scores.reshape(peer_count, arrived.shape[1], cent_count),
        "index",
        split_axis=0,
        concat_axis=0,
        tiled=True,
    )
    return jnp.dot(
        pick, returned.reshape(peer_count * owner_slots, cent_count),
        preferred_element_type=jnp.float32,
    ).astype(jnp.bfloat16)


def solution(mesh):
    return jax.shard_map(
        body,
        mesh=mesh,
        in_specs=(
            P(("graph", "index"), None),
            P(),
            P(),
            P(),
            P(),
            P(),
            P("index", None),
            P(("graph", "index"), None, None),
            P(("graph", "index"), None),
            P(("graph", "index"), None),
            P(("graph", "index"), None),
        ),
        out_specs=P(("graph", "index"), None),
        check_vma=False,
    )
```

```python
import jax
import jax.numpy as jnp
from jax import lax
from jax.sharding import PartitionSpec as P


def place_rows(label_rows, peer_count, owner_slots):
    hits = (label_rows[:, None] == jnp.arange(peer_count, dtype=jnp.int32)[None, :]).astype(
        jnp.int32
    )
    ranks = jnp.sum(hits * (jnp.cumsum(hits, axis=0) - 1), axis=1)
    return label_rows * owner_slots + ranks


def one_hot(index, count):
    return (index[:, None] == jnp.arange(count, dtype=jnp.int32)[None, :]).astype(jnp.bfloat16)


def body(
    features,
    q_weight,
    q_bias,
    w_self,
    w_neigh,
    z_bias,
    centroids,
    requests,
    slots,
    importance,
    labels,
):
    row_count = features.shape[0]
    width = features.shape[1]
    peer_count = lax.axis_size("index")
    owner_slots = max(2 * row_count // peer_count, 2)
    fetch_slots = requests.shape[2]
    slot_count = peer_count * fetch_slots
    cent_count = centroids.shape[0]
    wanted = lax.all_to_all(requests.astype(jnp.float32), "index", split_axis=1, concat_axis=1, tiled=True)[0].astype(jnp.int32)
    messages = jax.nn.relu(
        jnp.dot(features, q_weight, preferred_element_type=jnp.float32) + q_bias
    ).astype(jnp.bfloat16)
    weights_norm = importance / jnp.sum(importance, axis=1, keepdims=True)
    slot_ids = jnp.arange(slot_count, dtype=jnp.int32)
    mixing = jnp.sum(
        jnp.where(slots[:, :, None] == slot_ids[None, None, :], weights_norm[:, :, None], 0.0),
        axis=1,
    ).astype(jnp.bfloat16)
    outgoing_msgs = jnp.dot(
        one_hot(wanted.reshape(-1), row_count),
        lax.optimization_barrier(messages),
        preferred_element_type=jnp.float32,
    ).astype(jnp.bfloat16)
    fetched = lax.all_to_all(
        outgoing_msgs.reshape(peer_count, fetch_slots, width),
        "index",
        split_axis=0,
        concat_axis=0,
        tiled=True,
    ).reshape(slot_count, width)
    pooled = lax.optimization_barrier(
        jnp.dot(mixing, fetched, preferred_element_type=jnp.float32).astype(jnp.bfloat16))
    hidden = jax.nn.relu(
        jnp.dot(features, w_self, preferred_element_type=jnp.float32)
        + jnp.dot(pooled, w_neigh, preferred_element_type=jnp.float32)
        + z_bias
    )
    normed = (hidden * lax.rsqrt(jnp.mean(hidden * hidden, axis=1, keepdims=True) + 1e-06)).astype(
        jnp.bfloat16
    )
    positions = place_rows(labels[:, 0], peer_count, owner_slots)
    pick = one_hot(positions, peer_count * owner_slots)
    outgoing = lax.dot_general(
        pick, normed, (((0,), (0,)), ((), ())), preferred_element_type=jnp.float32
    ).astype(jnp.bfloat16)
    outgoing = outgoing.reshape(peer_count, owner_slots, width)
    arrived = lax.all_to_all(outgoing, "index", split_axis=0, concat_axis=0, tiled=True)
    flat_rows = arrived.reshape(-1, width)
    raw_scores = lax.dot_general(
        flat_rows, centroids, (((1,), (1,)), ((), ())), preferred_element_type=jnp.float32
    ).astype(jnp.bfloat16)
    returned = lax.all_to_all(
        raw_scores.reshape(peer_count, arrived.shape[1], cent_count),
        "index",
        split_axis=0,
        concat_axis=0,
        tiled=True,
    )
    return jnp.dot(
        pick, returned.reshape(peer_count * owner_slots, cent_count),
        preferred_element_type=jnp.float32,
    ).astype(jnp.bfloat16)


def solution(mesh):
    return jax.shard_map(
        body,
        mesh=mesh,
        in_specs=(
            P(("graph", "index"), None),
            P(),
            P(),
            P(),
            P(),
            P(),
            P("index", None),
            P(("graph", "index"), None, None),
            P(("graph", "index"), None),
            P(("graph", "index"), None),
            P(("graph", "index"), None),
        ),
        out_specs=P(("graph", "index"), None),
        check_vma=False,
    )
```

```python
import jax
import jax.numpy as jnp
from jax import lax
from jax.sharding import PartitionSpec as P


def place_rows(label_rows, peer_count, owner_slots):
    hits = (label_rows[:, None] == jnp.arange(peer_count, dtype=jnp.int32)[None, :]).astype(
        jnp.int32
    )
    ranks = jnp.sum(hits * (jnp.cumsum(hits, axis=0) - 1), axis=1)
    return label_rows * owner_slots + ranks


def one_hot(index, count):
    return (index[:, None] == jnp.arange(count, dtype=jnp.int32)[None, :]).astype(jnp.bfloat16)


def body(
    features,
    q_weight,
    q_bias,
    w_self,
    w_neigh,
    z_bias,
    centroids,
    requests,
    slots,
    importance,
    labels,
):
    row_count = features.shape[0]
    width = features.shape[1]
    peer_count = lax.axis_size("index")
    owner_slots = max(2 * row_count // peer_count, 2)
    fetch_slots = requests.shape[2]
    slot_count = peer_count * fetch_slots
    cent_count = centroids.shape[0]
    peer_eye = jnp.eye(peer_count, dtype=jnp.bfloat16)
    asked = jnp.dot(peer_eye, requests[0].astype(jnp.bfloat16), preferred_element_type=jnp.float32)
    wanted = lax.all_to_all(asked, "index", split_axis=0, concat_axis=0, tiled=True).astype(jnp.int32)
    messages = jax.nn.relu(
        jnp.dot(features, q_weight, preferred_element_type=jnp.float32) + q_bias
    ).astype(jnp.bfloat16)
    weights_norm = importance / jnp.sum(importance, axis=1, keepdims=True)
    slot_ids = jnp.arange(slot_count, dtype=jnp.int32)
    mixing = jnp.sum(
        jnp.where(slots[:, :, None] == slot_ids[None, None, :], weights_norm[:, :, None], 0.0),
        axis=1,
    ).astype(jnp.bfloat16)
    outgoing_msgs = jnp.dot(
        one_hot(wanted.reshape(-1), row_count),
        lax.optimization_barrier(messages),
        preferred_element_type=jnp.float32,
    ).astype(jnp.bfloat16)
    fetched = lax.all_to_all(
        outgoing_msgs.reshape(peer_count, fetch_slots, width),
        "index",
        split_axis=0,
        concat_axis=0,
        tiled=True,
    ).reshape(slot_count, width)
    pooled = lax.optimization_barrier(
        jnp.dot(mixing, fetched, preferred_element_type=jnp.float32).astype(jnp.bfloat16))
    hidden = jax.nn.relu(
        jnp.dot(features, w_self, preferred_element_type=jnp.float32)
        + jnp.dot(pooled, w_neigh, preferred_element_type=jnp.float32)
        + z_bias
    )
    normed = (hidden * lax.rsqrt(jnp.mean(hidden * hidden, axis=1, keepdims=True) + 1e-06)).astype(
        jnp.bfloat16
    )
    positions = place_rows(labels[:, 0], peer_count, owner_slots)
    pick = one_hot(positions, peer_count * owner_slots)
    outgoing = lax.dot_general(
        pick, normed, (((0,), (0,)), ((), ())), preferred_element_type=jnp.float32
    ).astype(jnp.bfloat16)
    outgoing = outgoing.reshape(peer_count, owner_slots, width)
    arrived = lax.all_to_all(outgoing, "index", split_axis=0, concat_axis=0, tiled=True)
    flat_rows = arrived.reshape(-1, width)
    raw_scores = lax.dot_general(
        flat_rows, centroids, (((1,), (1,)), ((), ())), preferred_element_type=jnp.float32
    ).astype(jnp.bfloat16)
    returned = lax.all_to_all(
        raw_scores.reshape(peer_count, arrived.shape[1], cent_count),
        "index",
        split_axis=0,
        concat_axis=0,
        tiled=True,
    )
    return jnp.dot(
        pick, returned.reshape(peer_count * owner_slots, cent_count),
        preferred_element_type=jnp.float32,
    ).astype(jnp.bfloat16)


def solution(mesh):
    return jax.shard_map(
        body,
        mesh=mesh,
        in_specs=(
            P(("graph", "index"), None),
            P(),
            P(),
            P(),
            P(),
            P(),
            P("index", None),
            P(("graph", "index"), None, None),
            P(("graph", "index"), None),
            P(("graph", "index"), None),
            P(("graph", "index"), None),
        ),
        out_specs=P(("graph", "index"), None),
        check_vma=False,
    )
```

```python
import jax
import jax.numpy as jnp
from jax import lax
from jax.sharding import PartitionSpec as P


def place_rows(label_rows, peer_count, owner_slots):
    hits = (label_rows[:, None] == jnp.arange(peer_count, dtype=jnp.int32)[None, :]).astype(
        jnp.int32
    )
    ranks = jnp.sum(hits * (jnp.cumsum(hits, axis=0) - 1), axis=1)
    return label_rows * owner_slots + ranks


def one_hot(index, count):
    return (index[:, None] == jnp.arange(count, dtype=jnp.int32)[None, :]).astype(jnp.bfloat16)


def body(
    features,
    q_weight,
    q_bias,
    w_self,
    w_neigh,
    z_bias,
    centroids,
    requests,
    slots,
    importance,
    labels,
):
    row_count = features.shape[0]
    width = features.shape[1]
    peer_count = lax.axis_size("index")
    owner_slots = max(2 * row_count // peer_count, 2)
    fetch_slots = requests.shape[2]
    slot_count = peer_count * fetch_slots
    cent_count = centroids.shape[0]
    peer_eye = jnp.eye(peer_count, dtype=jnp.bfloat16)
    asked = jnp.dot(peer_eye, requests[0].astype(jnp.bfloat16), preferred_element_type=jnp.float32)
    wanted = lax.all_to_all(asked, "index", split_axis=0, concat_axis=0, tiled=True)
    messages = jax.nn.relu(
        jnp.dot(features, q_weight, preferred_element_type=jnp.float32) + q_bias
    ).astype(jnp.bfloat16)
    weights_norm = importance / jnp.sum(importance, axis=1, keepdims=True)
    slot_ids = jnp.arange(slot_count, dtype=jnp.int32)
    mixing = jnp.sum(
        jnp.where(slots[:, :, None] == slot_ids[None, None, :], weights_norm[:, :, None], 0.0),
        axis=1,
    ).astype(jnp.bfloat16)
    outgoing_msgs = jnp.dot(
        (wanted.reshape(-1)[:, None] == jnp.arange(row_count, dtype=jnp.float32)[None, :]).astype(
            jnp.bfloat16
        ),
        lax.optimization_barrier(messages),
        preferred_element_type=jnp.float32,
    ).astype(jnp.bfloat16)
    fetched = lax.all_to_all(
        outgoing_msgs.reshape(peer_count, fetch_slots, width),
        "index",
        split_axis=0,
        concat_axis=0,
        tiled=True,
    ).reshape(slot_count, width)
    pooled = lax.optimization_barrier(
        jnp.dot(mixing, fetched, preferred_element_type=jnp.float32).astype(jnp.bfloat16))
    hidden = jax.nn.relu(
        jnp.dot(features, w_self, preferred_element_type=jnp.float32)
        + jnp.dot(pooled, w_neigh, preferred_element_type=jnp.float32)
        + z_bias
    )
    normed = (hidden * lax.rsqrt(jnp.mean(hidden * hidden, axis=1, keepdims=True) + 1e-06)).astype(
        jnp.bfloat16
    )
    positions = place_rows(labels[:, 0], peer_count, owner_slots)
    pick = one_hot(positions, peer_count * owner_slots)
    outgoing = lax.dot_general(
        pick, normed, (((0,), (0,)), ((), ())), preferred_element_type=jnp.float32
    ).astype(jnp.bfloat16)
    outgoing = outgoing.reshape(peer_count, owner_slots, width)
    arrived = lax.all_to_all(outgoing, "index", split_axis=0, concat_axis=0, tiled=True)
    flat_rows = arrived.reshape(-1, width)
    raw_scores = lax.dot_general(
        flat_rows, centroids, (((1,), (1,)), ((), ())), preferred_element_type=jnp.float32
    ).astype(jnp.bfloat16)
    returned = lax.all_to_all(
        raw_scores.reshape(peer_count, arrived.shape[1], cent_count),
        "index",
        split_axis=0,
        concat_axis=0,
        tiled=True,
    )
    return jnp.dot(
        pick, returned.reshape(peer_count * owner_slots, cent_count),
        preferred_element_type=jnp.float32,
    ).astype(jnp.bfloat16)


def solution(mesh):
    return jax.shard_map(
        body,
        mesh=mesh,
        in_specs=(
            P(("graph", "index"), None),
            P(),
            P(),
            P(),
            P(),
            P(),
            P("index", None),
            P(("graph", "index"), None, None),
            P(("graph", "index"), None),
            P(("graph", "index"), None),
            P(("graph", "index"), None),
        ),
        out_specs=P(("graph", "index"), None),
        check_vma=False,
    )
```
